512 devices in a mesh: mpo: 16 (over z), sec: 32 (over x, y, core).
Axes of the slice: x: 4, y: 4, z: 16, core: 2. Of those that a mesh axis runs over, the one named last changes fastest.
Arguments:
- environment: bfloat16 [48, 64, 128, 128], P('mpo', 'sec'), may hold values from -6 to 6
- site_tensor: bfloat16 [64, 4, 128, 128], P('sec'), may hold values from -0.25 to 0.25
- mpo_tensor: bfloat16 [48, 48, 4, 4], P('mpo'), may hold values from -0.75 to 0.75
- mpo_pattern: int32 [48, 48], P('mpo'), may hold values 0 or 1
- sector_rows: int32 [64], replicated, may hold values from 64 to 128
- sector_map: int32 [64], replicated, may hold values from 0 to 63, as said below
Outputs:
- new_environment: bfloat16 [48, 64, 128, 128], P('mpo', 'sec')
The draws below stay inside these ranges and needn't reach their ends.
Inputs may be any that keep to these rules, and one draw needn't show every extreme that they name: A permutation of the 64 sector labels: sector g takes the new label sector_map[g].
All inputs are finite; a program needn't handle non-finite values. No bound on the sum of `mpo_pattern` on one device may be relied on, other than what follows from the above.
Results may differ from the reference program's by a relative error of at most 0.02.
Values may be sent and summed in bfloat16 or wider, within the bound.
No kernel may reach another device: no remote copies, remote signals or barrier semaphores. Data moves between devices by JAX's collectives and lax.ppermute only.
A program may use at most 64 MiB of HBM per device.

```python
import jax
import jax.numpy as jnp
from jax import lax

BLOCK = 128
D_PHYS = 4
CH_DEV = 3
SEC_DEV = 2
W = 48
NSEC = 64
N_MPO = 16


def force_target(sigma, source, target):
    holder = jnp.argmax((sigma == target).astype(jnp.int32)).astype(jnp.int32)
    current = sigma[source]
    sigma = sigma.at[holder].set(current)
    return sigma.at[source].set(target)


def draw_sector_map(key, part):
    ranks = NSEC // SEC_DEV
    half = ranks // 2
    keys = jax.random.split(jax.random.fold_in(key, 7), SEC_DEV + 3)
    first = jax.random.randint(keys[0], (), 0, ranks, dtype=jnp.int32)
    step = 1 + jax.random.randint(keys[1], (), 0, ranks - 3, dtype=jnp.int32)
    step = jnp.where(step >= half - 1, step + 1, step)
    second = (first + step) % ranks
    columns = []
    for slot in range(SEC_DEV):
        sigma = jax.random.permutation(keys[2 + slot], ranks).astype(jnp.int32)
        if slot == 0:
            sigma = force_target(sigma, first, (first + half) % ranks)
            sigma = force_target(sigma, second, (second + 1) % ranks)
        columns.append(sigma)
    sigmas = jnp.stack(columns, axis=1)
    slot_keys = jax.random.split(keys[SEC_DEV + 2], ranks)
    taus = jax.vmap(lambda k: jax.random.permutation(k, SEC_DEV).astype(jnp.int32))(slot_keys)
    slots = jnp.arange(SEC_DEV, dtype=jnp.int32)
    new_slot = taus[sigmas, slots[None, :]]
    return (sigmas * SEC_DEV + new_slot).reshape(NSEC).astype(jnp.int32)


def place_ends(drawn, stream_key, least, top_value):
    spot = [jax.random.randint(jax.random.fold_in(stream_key, axis), (), 0, length) for axis, length in enumerate(drawn.shape)]
    longest = drawn.shape.index(max(drawn.shape))
    beside = spot[:longest] + [(spot[longest] + 1) % drawn.shape[longest]] + spot[longest + 1:]
    return drawn.at[tuple(spot)].set(least).at[tuple(beside)].set(top_value)


def steps_of(stream_key, dims, cuts, low, largest):
    def one(axis_at, parts):
        heights = jax.random.uniform(jax.random.fold_in(jax.random.fold_in(stream_key, 6), axis_at), (parts,), jnp.float32, low / len(cuts), largest / len(cuts))
        return jnp.repeat(jnp.exp(heights), dims[axis_at] // parts).reshape((-1,) + (1,) * (len(dims) - axis_at - 1))

    factor_of = one(*cuts[0])
    for cut in cuts[1:]:
        factor_of = factor_of * one(*cut)
    return factor_of


def gaussian(key, extent, width, limit, shards=(), held_as=jnp.bfloat16):
    loudness = steps_of(key, extent, shards, -0.22, 0.18) if shards else 1.0
    array = jax.random.normal(key, extent, jnp.float32) * width * loudness
    return jnp.minimum(jnp.maximum(array, -limit), limit).astype(held_as)


def setup_inputs(seed: int = 0) -> dict:
    key_of = jax.random.split(jax.random.key(seed), 7)
    return {
        "environment": gaussian(key_of[0], (W, NSEC, BLOCK, BLOCK), 1.0, 6.0, ((0, 16), (1, 32))),
        "site_tensor": gaussian(key_of[1], (NSEC, D_PHYS, BLOCK, BLOCK), (D_PHYS * BLOCK) ** -0.5, 0.25, ((0, 32),)),
        "mpo_tensor": gaussian(key_of[2], (W, W, D_PHYS, D_PHYS), (W * D_PHYS // 3) ** -0.5, 0.75, ((0, 16),)),
        "mpo_pattern": place_ends((jax.random.randint(key_of[3], (W, W), 0, 3) < 1).astype(jnp.int32), jax.random.fold_in(key_of[3], 1), 0, 1),
        "sector_rows": place_ends(jax.random.randint(key_of[4], (NSEC,), BLOCK // 2, BLOCK + 1), jax.random.fold_in(key_of[4], 1), BLOCK // 2, BLOCK).astype(jnp.int32),
        "sector_map": draw_sector_map(jax.random.fold_in(key_of[6], 71), 0),
    }


def reference(environment, site_tensor, mpo_tensor, mpo_pattern, sector_rows, sector_map):
    masked = jnp.where(mpo_pattern[:, :, None, None] != 0, mpo_tensor, jnp.zeros_like(mpo_tensor))
    mgroups = masked.reshape(N_MPO, CH_DEV, W, D_PHYS, D_PHYS)

    def one_sector(index):
        env = lax.dynamic_index_in_dim(environment, index, 1, keepdims=False).astype(jnp.float32)
        site = lax.dynamic_index_in_dim(site_tensor, index, 0, keepdims=False).astype(jnp.float32)
        attached = jnp.einsum("bac,tcz->btaz", env, site).astype(jnp.bfloat16)
        agroups = attached.reshape(N_MPO, CH_DEV, D_PHYS, BLOCK, BLOCK)

        def one_group(total, pieces):
            weight_group, attach_group = pieces
            mixed = jnp.einsum("bpst,btaz->psaz", weight_group.astype(jnp.float32), attach_group.astype(jnp.float32))
            mixed = lax.optimization_barrier(mixed.astype(jnp.bfloat16)).astype(jnp.float32)
            part = jnp.einsum("sxa,psxz->paz", site, mixed)
            part = lax.optimization_barrier(part.astype(jnp.bfloat16)).astype(jnp.float32)
            return total + part, None

        start = jnp.zeros((W, BLOCK, BLOCK), jnp.float32)
        total, unused = lax.scan(one_group, start, (mgroups, agroups))
        return total.astype(jnp.bfloat16)

    summed = lax.map(one_sector, jnp.arange(NSEC, dtype=jnp.int32))
    places = jnp.arange(BLOCK, dtype=jnp.int32)
    keep = (places[None, :, None] < sector_rows[:, None, None]) & (places[None, None, :] < sector_rows[:, None, None])
    masked_out = jnp.where(keep[:, None, :, :], summed, jnp.zeros_like(summed))
    placed = jnp.zeros_like(masked_out).at[sector_map.astype(jnp.int32)].set(masked_out)
    return jnp.transpose(placed, (1, 0, 2, 3))
```

```python
import jax
import jax.numpy as jnp
from jax import lax
from jax.sharding import PartitionSpec as P


def per_device(environment, site_tensor, mpo_tensor, mpo_pattern, sector_rows, sector_map):
    per_dev = environment.shape[1]
    block = environment.shape[2]
    masked = jnp.where(mpo_pattern[:, :, None, None] != 0, mpo_tensor, jnp.zeros_like(mpo_tensor))
    left = jnp.einsum(
        "gsxa,bgxc->gbsac", site_tensor, environment, preferred_element_type=jnp.float32
    ).astype(jnp.bfloat16)
    sandwich = jnp.einsum(
        "gbsac,gtcz->bstgaz", left, site_tensor, preferred_element_type=jnp.float32
    ).astype(jnp.bfloat16)
    parts = jnp.einsum(
        "bpst,bstgaz->pgaz", masked, sandwich, preferred_element_type=jnp.float32
    ).astype(jnp.bfloat16)
    summed = lax.psum_scatter(parts, "mpo", scatter_dimension=0, tiled=True)
    device = lax.axis_index("sec")
    local = jnp.arange(per_dev, dtype=jnp.int32)
    own_labels = device * per_dev + local
    sizes = jnp.take(sector_rows, own_labels, axis=0)
    places = jnp.arange(block, dtype=jnp.int32)
    keep = (places[None, :, None] < sizes[:, None, None]) & (
        places[None, None, :] < sizes[:, None, None]
    )
    result = jnp.where(keep[None, :, :, :], summed, jnp.zeros_like(summed))
    gathered = lax.all_gather(result, "sec", axis=1, tiled=True)
    nsec = sector_map.shape[0]
    inverse = jnp.zeros((nsec,), jnp.int32).at[sector_map].set(jnp.arange(nsec, dtype=jnp.int32))
    source = jnp.take(inverse, own_labels, axis=0)
    return jnp.take(gathered, source, axis=1)


def solution(mesh):
    return jax.shard_map(
        per_device,
        mesh=mesh,
        in_specs=(
            P("mpo", "sec", None, None),
            P("sec", None, None, None),
            P("mpo", None, None, None),
            P("mpo", None),
            P(),
            P(),
        ),
        out_specs=P("mpo", "sec", None, None),
        check_vma=False,
    )
```

```python
import jax
import jax.numpy as jnp
from jax import lax
from jax.sharding import PartitionSpec as P


def per_device(environment, site_tensor, mpo_tensor, mpo_pattern, sector_rows, sector_map):
    channels, per_dev, block = environment.shape[0], environment.shape[1], environment.shape[2]
    nsec = sector_map.shape[0]
    device = lax.axis_index("sec")
    local = jnp.arange(per_dev, dtype=jnp.int32)
    own_labels = device * per_dev + local
    inverse = jnp.zeros((nsec,), jnp.int32).at[sector_map].set(jnp.arange(nsec, dtype=jnp.int32))
    source = jnp.take(inverse, own_labels, axis=0)
    sizes = jnp.take(sector_rows, source, axis=0)

    masked = jnp.where(mpo_pattern[:, :, None, None] != 0, mpo_tensor, jnp.zeros_like(mpo_tensor))
    left = jnp.einsum(
        "gsxa,bgxc->gbsac", site_tensor, environment, preferred_element_type=jnp.float32
    ).astype(jnp.bfloat16)
    sandwich = jnp.einsum(
        "gbsac,gtcz->bstgaz", left, site_tensor, preferred_element_type=jnp.float32
    ).astype(jnp.bfloat16)
    parts = jnp.einsum(
        "bpst,bstgaz->pgaz", masked, sandwich, preferred_element_type=jnp.float32
    ).astype(jnp.bfloat16)
    summed = lax.psum_scatter(parts, "mpo", scatter_dimension=0, tiled=True)
    gathered = lax.all_gather(summed, "sec", axis=1, tiled=True)
    places = jnp.arange(block, dtype=jnp.int32)
    picked = []
    for k in range(per_dev):
        one = lax.dynamic_index_in_dim(gathered, source[k], axis=1, keepdims=False)
        keep = (places[:, None] < sizes[k]) & (places[None, :] < sizes[k])
        picked.append(jnp.where(keep[None], one, jnp.zeros_like(one)))
    return jnp.stack(picked, axis=1)


def solution(mesh):
    return jax.shard_map(
        per_device,
        mesh=mesh,
        in_specs=(
            P("mpo", "sec", None, None),
            P("sec", None, None, None),
            P("mpo", None, None, None),
            P("mpo", None),
            P(),
            P(),
        ),
        out_specs=P("mpo", "sec", None, None),
        check_vma=False,
    )
```

```python
import jax
import jax.numpy as jnp
from jax import lax
from jax.sharding import PartitionSpec as P


def per_device(environment, site_tensor, mpo_tensor, mpo_pattern, sector_rows, sector_map):
    channels, per_dev, block = environment.shape[0], environment.shape[1], environment.shape[2]
    nsec = sector_map.shape[0]
    device = lax.axis_index("sec")
    local = jnp.arange(per_dev, dtype=jnp.int32)
    own_labels = device * per_dev + local
    hit = sector_map[None, :] == own_labels[:, None]
    labels = jnp.arange(nsec, dtype=jnp.int32)
    source = jnp.sum(jnp.where(hit, labels[None, :], 0), axis=1)
    sizes = jnp.sum(jnp.where(hit, sector_rows[None, :], 0), axis=1)

    masked = jnp.where(mpo_pattern[:, :, None, None] != 0, mpo_tensor, jnp.zeros_like(mpo_tensor))
    left = jnp.einsum(
        "gsxa,bgxc->gbsac", site_tensor, environment, preferred_element_type=jnp.float32
    ).astype(jnp.bfloat16)
    sandwich = jnp.einsum(
        "gbsac,gtcz->bstgaz", left, site_tensor, preferred_element_type=jnp.float32
    ).astype(jnp.bfloat16)
    parts = jnp.einsum(
        "bpst,bstgaz->pgaz", masked, sandwich, preferred_element_type=jnp.float32
    ).astype(jnp.bfloat16)
    summed = lax.psum_scatter(parts, "mpo", scatter_dimension=0, tiled=True)
    gathered = lax.all_gather(summed, "sec", axis=1, tiled=True)
    places = jnp.arange(block, dtype=jnp.int32)
    picked = []
    for k in range(per_dev):
        one = lax.dynamic_index_in_dim(gathered, source[k], axis=1, keepdims=False)
        keep = (places[:, None] < sizes[k]) & (places[None, :] < sizes[k])
        picked.append(jnp.where(keep[None], one, jnp.zeros_like(one)))
    return jnp.stack(picked, axis=1)


def solution(mesh):
    return jax.shard_map(
        per_device,
        mesh=mesh,
        in_specs=(
            P("mpo", "sec", None, None),
            P("sec", None, None, None),
            P("mpo", None, None, None),
            P("mpo", None),
            P(),
            P(),
        ),
        out_specs=P("mpo", "sec", None, None),
        check_vma=False,
    )
```

```python
import jax
import jax.numpy as jnp
from jax import lax
from jax.sharding import PartitionSpec as P


def per_device(environment, site_tensor, mpo_tensor, mpo_pattern, sector_rows, sector_map):
    channels, per_dev, block = environment.shape[0], environment.shape[1], environment.shape[2]
    nsec = sector_map.shape[0]
    device = lax.axis_index("sec")
    local = jnp.arange(per_dev, dtype=jnp.int32)
    own_labels = device * per_dev + local
    hit = sector_map[None, :] == own_labels[:, None]
    labels = jnp.arange(nsec, dtype=jnp.int32)
    source = jnp.sum(jnp.where(hit, labels[None, :], 0), axis=1)
    sizes = jnp.sum(jnp.where(hit, sector_rows[None, :], 0), axis=1)

    masked = jnp.where(mpo_pattern[:, :, None, None] != 0, mpo_tensor, jnp.zeros_like(mpo_tensor))
    left = jnp.einsum(
        "gsxa,bgxc->gbsac", site_tensor, environment, preferred_element_type=jnp.float32
    ).astype(jnp.bfloat16)
    sandwich = jnp.einsum(
        "gbsac,gtcz->bstgaz", left, site_tensor, preferred_element_type=jnp.float32
    ).astype(jnp.bfloat16)
    parts = jnp.einsum(
        "bpst,bstgaz->pgaz", masked, sandwich, preferred_element_type=jnp.float32
    ).astype(jnp.bfloat16)
    summed = lax.psum_scatter(parts, "mpo", scatter_dimension=0, tiled=True)
    summed, source, sizes = lax.optimization_barrier((summed, source, sizes))
    gathered = lax.all_gather(summed[None], "sec", axis=0, tiled=True)
    places = jnp.arange(block, dtype=jnp.int32)
    picked = []
    for k in range(per_dev):
        one = lax.dynamic_slice(
            gathered,
            (source[k] // per_dev, 0, source[k] % per_dev, 0, 0),
            (1, channels, 1, block, block),
        ).reshape(channels, block, block)
        keep = (places[:, None] < sizes[k]) & (places[None, :] < sizes[k])
        picked.append(jnp.where(keep[None], one, jnp.zeros_like(one)))
    return jnp.stack(picked, axis=1)


def solution(mesh):
    return jax.shard_map(
        per_device,
        mesh=mesh,
        in_specs=(
            P("mpo", "sec", None, None),
            P("sec", None, None, None),
            P("mpo", None, None, None),
            P("mpo", None),
            P(),
            P(),
        ),
        out_specs=P("mpo", "sec", None, None),
        check_vma=False,
    )
```

```python
import jax
import jax.numpy as jnp
from jax import lax
from jax.sharding import PartitionSpec as P


def per_device(environment, site_tensor, mpo_tensor, mpo_pattern, sector_rows, sector_map):
    channels, per_dev, block = environment.shape[0], environment.shape[1], environment.shape[2]
    nsec = sector_map.shape[0]
    device = lax.axis_index("sec")
    local = jnp.arange(per_dev, dtype=jnp.int32)
    own_labels = device * per_dev + local
    hit = sector_map[None, :] == own_labels[:, None]
    labels = jnp.arange(nsec, dtype=jnp.int32)
    source = jnp.sum(jnp.where(hit, labels[None, :], 0), axis=1)
    sizes = jnp.take(sector_rows, own_labels, axis=0)

    masked = jnp.where(mpo_pattern[:, :, None, None] != 0, mpo_tensor, jnp.zeros_like(mpo_tensor))
    left = jnp.einsum(
        "gsxa,bgxc->gbsac", site_tensor, environment, preferred_element_type=jnp.float32
    ).astype(jnp.bfloat16)
    sandwich = jnp.einsum(
        "gbsac,gtcz->bstgaz", left, site_tensor, preferred_element_type=jnp.float32
    ).astype(jnp.bfloat16)
    parts = jnp.einsum(
        "bpst,bstgaz->pgaz", masked, sandwich, preferred_element_type=jnp.float32
    ).astype(jnp.bfloat16)
    summed = lax.psum_scatter(parts, "mpo", scatter_dimension=0, tiled=True)
    places = jnp.arange(block, dtype=jnp.int32)
    keep = (places[None, :, None] < sizes[:, None, None]) & (
        places[None, None, :] < sizes[:, None, None]
    )
    summed = jnp.where(keep[None], summed, jnp.zeros_like(summed))
    gathered = lax.all_gather(summed[None], "sec", axis=0, tiled=True)
    picked = [
        lax.dynamic_slice(
            gathered,
            (source[k] // per_dev, 0, source[k] % per_dev, 0, 0),
            (1, channels, 1, block, block),
        )[0]
        for k in range(per_dev)
    ]
    return jnp.concatenate(picked, axis=1)


def solution(mesh):
    return jax.shard_map(
        per_device,
        mesh=mesh,
        in_specs=(
            P("mpo", "sec", None, None),
            P("sec", None, None, None),
            P("mpo", None, None, None),
            P("mpo", None),
            P(),
            P(),
        ),
        out_specs=P("mpo", "sec", None, None),
        check_vma=False,
    )
```

```python
import jax
import jax.numpy as jnp
from jax import lax
from jax.sharding import PartitionSpec as P


def per_device(environment, site_tensor, mpo_tensor, mpo_pattern, sector_rows, sector_map):
    channels, per_dev, block = environment.shape[0], environment.shape[1], environment.shape[2]
    nsec = sector_map.shape[0]
    device = lax.axis_index("sec")
    local = jnp.arange(per_dev, dtype=jnp.int32)
    own_labels = device * per_dev + local
    hit = sector_map[None, :] == own_labels[:, None]
    labels = jnp.arange(nsec, dtype=jnp.int32)
    source = jnp.sum(jnp.where(hit, labels[None, :], 0), axis=1)
    sizes = jnp.sum(jnp.where(hit, sector_rows[None, :], 0), axis=1)

    masked = mpo_tensor * mpo_pattern.astype(mpo_tensor.dtype)[:, :, None, None]
    left = jnp.einsum(
        "gsxa,bgxc->gbsac", site_tensor, environment, preferred_element_type=jnp.float32
    ).astype(jnp.bfloat16)
    sandwich = jnp.einsum(
        "gbsac,gtcz->bstgaz", left, site_tensor, preferred_element_type=jnp.float32
    ).astype(jnp.bfloat16)
    parts = jnp.einsum(
        "bpst,bstgaz->pgaz", masked, sandwich, preferred_element_type=jnp.float32
    ).astype(jnp.bfloat16)
    summed = lax.psum_scatter(parts, "mpo", scatter_dimension=0, tiled=True)
    gathered = lax.all_gather(summed, "sec", axis=1, tiled=True)
    places = jnp.arange(block, dtype=jnp.int32)
    picked = []
    for k in range(per_dev):
        one = lax.dynamic_index_in_dim(gathered, source[k], axis=1, keepdims=False)
        keep = (places[:, None] < sizes[k]) & (places[None, :] < sizes[k])
        picked.append(jnp.where(keep[None], one, jnp.zeros_like(one)))
    return jnp.stack(picked, axis=1)


def solution(mesh):
    return jax.shard_map(
        per_device,
        mesh=mesh,
        in_specs=(
            P("mpo", "sec", None, None),
            P("sec", None, None, None),
            P("mpo", None, None, None),
            P("mpo", None),
            P(),
            P(),
        ),
        out_specs=P("mpo", "sec", None, None),
        check_vma=False,
    )
```
